512 devices in a mesh: ctx: 64 (over x, z), ch: 8 (over y, core).
Axes of the slice: x: 4, y: 4, z: 16, core: 2. Of those that a mesh axis runs over, the one named last changes fastest.
Arguments:
- conv_input: bfloat16 [8192, 4096], P('ctx', 'ch'), may hold values from -6 to 6
- residues: float32 [4096, 16], P('ch'), may hold values from -4 to 4
- decay_rates: float32 [4096, 16], P('ch'), as said below
- skip_gain: float32 [4096], P('ch'), may hold values from -1 to 1
- query_rows: bfloat16 [8192, 4096], P('ctx', 'ch'), may hold values from -5 to 5
- key_rows: bfloat16 [8192, 4096], P('ctx', 'ch'), may hold values from -5 to 5
- value_rows: bfloat16 [8192, 4096], P('ctx', 'ch'), may hold values from -16 to 16
- norm_gain: float32 [4096], P('ch'), may hold values from 0.5 to 1.5
Outputs:
- conv_out: bfloat16 [8192, 4096], P('ctx', 'ch')
- attended: bfloat16 [8192, 4096], P('ctx', 'ch')
The draws below stay inside these ranges and needn't reach their ends.
Inputs may be any that keep to these rules, and one draw needn't show every extreme that they name: `decay_rates`: decay rates lie between 0.5 / 8192 and 1 / 30.
All inputs are finite; a program needn't handle non-finite values.
Results may differ from the reference program's by a relative error of at most 0.019.
Values may be sent and summed in bfloat16 or wider, within the bound.
No kernel may reach another device: no remote copies, remote signals or barrier semaphores. Data moves between devices by JAX's collectives and lax.ppermute only.
A program may use at most 64 MiB of HBM per device.

```python
import math
import jax
import jax.numpy as jnp
from jax import lax

HEADS = 32
HD = 128
MODES = 16
TOK_DEV = 128
SEQ = 8192
WIDTH = 4096
CH = 4096
N_CTX = 64


def draw_decay_rates(key, part):
    lowest = math.log(0.5 / SEQ)
    highest = math.log(1.0 / 30.0)
    unit_draw = jax.random.uniform(key, (CH, MODES), jnp.float32)
    return jnp.exp(lowest + (highest - lowest) * unit_draw)


def attention_tables(key):
    query_seed = jax.random.fold_in(key, 101)
    key_seed = jax.random.fold_in(key, 202)
    table_shape = (SEQ, HEADS * HD)
    query_table = jnp.clip(jax.random.normal(query_seed, table_shape, jnp.float32), -5.0, 5.0)
    key_table = jnp.clip(jax.random.normal(key_seed, table_shape, jnp.float32), -5.0, 5.0)
    return (query_table, key_table)


def draw_query_rows(key, part):
    return attention_tables(key)[0].astype(jnp.bfloat16)


def draw_key_rows(key, part):
    return attention_tables(key)[1].astype(jnp.bfloat16)


def draw_value_rows(key, part):
    table_shape = (SEQ, HEADS * HD)
    column = jnp.arange(HEADS * HD, dtype=jnp.float32) / (HEADS * HD - 1)
    base_seed = jax.random.fold_in(key, 404)
    base_table = jnp.clip(jax.random.normal(base_seed, table_shape, jnp.float32), -5.0, 5.0)
    growth = jnp.exp(math.log(3.0) * column)
    return (base_table * growth[None, :]).astype(jnp.bfloat16)


def block_levels(key, extent, shards, smallest, largest):
    def one(axis_at, blocks):
        heights = jax.random.uniform(jax.random.fold_in(jax.random.fold_in(key, 6), axis_at), (blocks,), jnp.float32, smallest / len(shards), largest / len(shards))
        return jnp.repeat(jnp.exp(heights), extent[axis_at] // blocks).reshape((-1,) + (1,) * (len(extent) - axis_at - 1))

    gain = one(*shards[0])
    for cut in shards[1:]:
        gain = gain * one(*cut)
    return gain


def noise(own_key, dims, deviation, limit, cuts=(), held_as=jnp.bfloat16):
    loudness = block_levels(own_key, dims, cuts, -0.22, 0.18) if cuts else 1.0
    values = jax.random.normal(own_key, dims, jnp.float32) * deviation * loudness
    return jnp.minimum(jnp.maximum(values, -limit), limit).astype(held_as)


def setup_inputs(seed: int = 0) -> dict:
    key_of = jax.random.split(jax.random.key(seed), 9)
    return {
        "conv_input": noise(key_of[0], (SEQ, CH), 1.0, 6.0, ((0, 64), (1, 8))),
        "residues": noise(key_of[1], (CH, MODES), 0.25, 4.0, ((0, 8),), jnp.float32),
        "decay_rates": draw_decay_rates(jax.random.fold_in(key_of[8], 71), 0),
        "skip_gain": jnp.clip(jax.random.uniform(key_of[3], (CH,), jnp.float32, -1.0, 1.0) * block_levels(key_of[3], (CH,), ((0, 8),), -0.4, 0.0), -1.0, 1.0),
        "query_rows": draw_query_rows(jax.random.fold_in(key_of[8], 71), 0),
        "key_rows": draw_key_rows(jax.random.fold_in(key_of[8], 71), 0),
        "value_rows": draw_value_rows(jax.random.fold_in(key_of[8], 71), 0),
        "norm_gain": jnp.clip(1.0 + 0.1 * jax.random.normal(key_of[7], (WIDTH,), jnp.float32), 0.5, 1.5),
    }


def attend_block(block_index, query_rows, key_padded, value_padded):
    start_row = block_index * TOK_DEV
    query_block = lax.dynamic_slice_in_dim(query_rows, start_row, TOK_DEV, 0).astype(jnp.float32).reshape(TOK_DEV, HEADS, HD)
    key_block = lax.dynamic_slice_in_dim(key_padded, start_row, 2 * TOK_DEV, 0).astype(jnp.float32).reshape(2 * TOK_DEV, HEADS, HD)
    value_block = lax.dynamic_slice_in_dim(value_padded, start_row, 2 * TOK_DEV, 0).astype(jnp.float32).reshape(2 * TOK_DEV, HEADS, HD)
    scores = jnp.einsum('qhd,khd->hqk', query_block, key_block) * HD ** (-0.5)
    query_place = jnp.arange(TOK_DEV, dtype=jnp.int32)[:, None]
    key_place = jnp.arange(2 * TOK_DEV, dtype=jnp.int32)[None, :] - TOK_DEV
    allowed = (key_place <= query_place) & ((key_place >= 0) | (block_index > 0))
    scores = jnp.where(allowed[None], scores, -jnp.inf)
    row_max = lax.optimization_barrier(jnp.max(scores, axis=-1, keepdims=True))
    weights = jnp.exp(scores - row_max)
    row_total = lax.optimization_barrier(jnp.sum(weights, axis=-1))
    rounded = weights.astype(jnp.bfloat16).astype(jnp.float32)
    mixed_heads = jnp.einsum('hqk,khd->qhd', rounded, value_block)
    mixed_heads = mixed_heads / jnp.transpose(row_total)[:, :, None]
    return mixed_heads.reshape(TOK_DEV, WIDTH).astype(jnp.bfloat16)

def reference(conv_input, residues, decay_rates, skip_gain, query_rows, key_rows, value_rows, norm_gain):
    signal = conv_input.astype(jnp.float32)
    step_axis = jnp.arange(SEQ, dtype=jnp.float32)[:, None]
    kernel = jnp.zeros((SEQ, CH), jnp.float32)
    for mode_index in range(MODES):
        decay_rate = decay_rates[:, mode_index]
        weight = residues[:, mode_index] * jnp.sqrt(-jnp.expm1(-decay_rate) * (1.0 + jnp.exp(-decay_rate)))
        kernel = kernel + weight[None, :] * jnp.exp(-decay_rate[None, :] * step_axis)
    spectrum = jnp.fft.rfft(signal, n=2 * SEQ, axis=0) * jnp.fft.rfft(kernel, n=2 * SEQ, axis=0)
    convolved = jnp.fft.irfft(spectrum, n=2 * SEQ, axis=0)[:SEQ]
    conv_out = (convolved + skip_gain[None, :] * signal).astype(jnp.bfloat16)
    gated = (value_rows.astype(jnp.float32) * conv_out.astype(jnp.float32)).astype(jnp.bfloat16)
    zero_block = jnp.zeros((TOK_DEV, WIDTH), jnp.bfloat16)
    key_padded = jnp.concatenate([zero_block, key_rows], axis=0)
    value_padded = jnp.concatenate([zero_block, gated], axis=0)
    blocks = lax.map(lambda block_index: attend_block(block_index, query_rows, key_padded, value_padded), jnp.arange(N_CTX, dtype=jnp.int32))
    attention = blocks.reshape(SEQ, WIDTH)
    attention_wide = attention.astype(jnp.float32)
    mean_square = lax.optimization_barrier(jnp.mean(attention_wide * attention_wide, axis=1))
    attended = (attention_wide * norm_gain[None, :] / jnp.sqrt(mean_square + 1e-06)[:, None]).astype(jnp.bfloat16)
    return (conv_out, attended)
```

```python
import jax
import jax.numpy as jnp
from jax import lax
from jax.sharding import PartitionSpec as P

HD = 128


def partner_2(value, axis, apart):
    mask = 2**apart
    pairs = [(source, source ^ mask) for source in range(lax.axis_size(axis))]
    return lax.ppermute(value, axis, pairs)


def shifted(block, axis, distance):
    devices = range(lax.axis_size(axis))
    route = [(i - distance, i) for i in devices if i - distance in devices]
    return lax.ppermute(block, axis, route)


def per_device(
    conv_input, residues, decay_rates, skip_gain, query_rows, key_rows, value_rows, norm_gain
):
    ctx_count = lax.axis_size("ctx")
    ch_count = lax.axis_size("ch")
    position = lax.axis_index("ctx")
    row_count, chan_count = conv_input.shape
    signal = conv_input.astype(jnp.float32)
    rates = jnp.transpose(decay_rates)
    weight = jnp.transpose(residues) * jnp.sqrt(-jnp.expm1(-rates) * (1.0 + jnp.exp(-rates)))
    steps = jnp.arange(row_count, dtype=jnp.float32)
    last = float(row_count - 1)

    tail = jnp.exp(-rates[:, None, :] * (last - steps)[None, :, None])
    own_state = jnp.sum(tail * signal[None], axis=1)

    before = jnp.zeros_like(own_state)
    span = 1
    while span < ctx_count:
        sent = own_state + before
        got = shifted(sent, "ctx", span)
        before = before + jnp.exp(-rates * float(row_count * span)) * got
        span *= 2

    rise = jnp.exp(rates[:, None, :] * steps[None, :, None])
    lifted = rise * signal[None]
    lifted_hi = lifted.astype(jnp.bfloat16)
    lifted_lo = (lifted - lifted_hi.astype(jnp.float32)).astype(jnp.bfloat16)
    lower = (steps[:, None] >= steps[None, :]).astype(jnp.bfloat16)
    prefix = jnp.einsum(
        "ts,rsc->rtc", lower, lifted_hi, preferred_element_type=jnp.float32
    ) + jnp.einsum("ts,rsc->rtc", lower, lifted_lo, preferred_element_type=jnp.float32)

    fall = weight[:, None, :] * jnp.exp(-rates[:, None, :] * steps[None, :, None])
    carried = jnp.exp(rates * last) * before
    convolved = jnp.sum(fall * (prefix + carried[:, None, :]), axis=0)
    conv_out = (convolved + skip_gain[None, :] * signal).astype(jnp.bfloat16)
    gated = (value_rows.astype(jnp.float32) * conv_out.astype(jnp.float32)).astype(jnp.bfloat16)

    heads_here = query_rows.shape[1] // HD
    previous_keys = shifted(key_rows, "ctx", 1)
    previous_gated = shifted(gated, "ctx", 1)
    key_window = jnp.concatenate([previous_keys, key_rows], axis=0).reshape(
        2 * row_count, heads_here, HD
    )
    value_window = jnp.concatenate([previous_gated, gated], axis=0).reshape(
        2 * row_count, heads_here, HD
    )
    query_heads = query_rows.reshape(row_count, heads_here, HD)
    scores = jnp.einsum(
        "qhd,khd->hqk", query_heads, key_window, preferred_element_type=jnp.float32
    ) * HD ** (-0.5)
    query_place = jnp.arange(row_count, dtype=jnp.int32)[:, None]
    key_place = jnp.arange(2 * row_count, dtype=jnp.int32)[None, :] - row_count
    allowed = (key_place <= query_place) & ((key_place >= 0) | (position > 0))
    scores = jnp.where(allowed[None], scores, -jnp.inf)
    row_max = jnp.max(scores, axis=-1, keepdims=True)
    weights = jnp.exp(scores - row_max)
    row_total = jnp.sum(weights, axis=-1)
    mixed_heads = jnp.einsum(
        "hqk,khd->qhd",
        weights.astype(jnp.bfloat16),
        value_window,
        preferred_element_type=jnp.float32,
    )
    mixed_heads = mixed_heads / jnp.transpose(row_total)[:, :, None]
    attention = mixed_heads.reshape(row_count, heads_here * HD).astype(jnp.bfloat16)
    attention_wide = attention.astype(jnp.float32)
    energy = jnp.sum(attention_wide * attention_wide, axis=1)
    for bit_index in range(ch_count.bit_length() - 1):
        energy = energy + partner_2(energy, "ch", bit_index)
    mean_square = energy / float(query_rows.shape[1] * ch_count)
    attended = (
        attention_wide * norm_gain[None, :] / jnp.sqrt(mean_square + 1e-06)[:, None]
    ).astype(jnp.bfloat16)
    return (conv_out, attended)


def solution(mesh):
    return jax.shard_map(
        per_device,
        mesh=mesh,
        in_specs=(
            P("ctx", "ch"),
            P("ch", None),
            P("ch", None),
            P("ch"),
            P("ctx", "ch"),
            P("ctx", "ch"),
            P("ctx", "ch"),
            P("ch"),
        ),
        out_specs=(P("ctx", "ch"), P("ctx", "ch")),
        check_vma=False,
    )
```

```python
import jax
import jax.numpy as jnp
from jax import lax
from jax.sharding import PartitionSpec as P

HD = 128
RADIX = 8


def rotated(value, axis, distance):
    count = lax.axis_size(axis)
    return lax.ppermute(value, axis, [(i, (i + distance) % count) for i in range(count)])


def shifted(block, axis, distance):
    devices = range(lax.axis_size(axis))
    route = [(i - distance, i) for i in devices if i - distance in devices]
    return lax.ppermute(block, axis, route)


def per_device(
    conv_input, residues, decay_rates, skip_gain, query_rows, key_rows, value_rows, norm_gain
):
    ctx_count = lax.axis_size("ctx")
    ch_count = lax.axis_size("ch")
    position = lax.axis_index("ctx")
    row_count, chan_count = conv_input.shape
    signal = conv_input.astype(jnp.float32)
    rates = jnp.transpose(decay_rates)
    weight = jnp.transpose(residues) * jnp.sqrt(-jnp.expm1(-rates) * (1.0 + jnp.exp(-rates)))
    steps = jnp.arange(row_count, dtype=jnp.float32)
    last = float(row_count - 1)

    tail = jnp.exp(-rates[:, None, :] * (last - steps)[None, :, None])
    own_state = jnp.sum(tail * signal[None], axis=1)

    before = jnp.zeros_like(own_state)
    span = 1
    while span < ctx_count:
        sent = own_state + before
        gathered = before
        for step in range(1, RADIX):
            if step * span < ctx_count:
                got = shifted(sent, "ctx", step * span)
                gathered = gathered + jnp.exp(-rates * float(row_count * span * step)) * got
        before = gathered
        span *= RADIX

    rise = jnp.exp(rates[:, None, :] * steps[None, :, None])
    lifted = rise * signal[None]
    lifted_hi = lifted.astype(jnp.bfloat16)
    lifted_lo = (lifted - lifted_hi.astype(jnp.float32)).astype(jnp.bfloat16)
    lower = (steps[:, None] >= steps[None, :]).astype(jnp.bfloat16)
    prefix = jnp.einsum(
        "ts,rsc->rtc", lower, lifted_hi, preferred_element_type=jnp.float32
    ) + jnp.einsum("ts,rsc->rtc", lower, lifted_lo, preferred_element_type=jnp.float32)

    fall = weight[:, None, :] * jnp.exp(-rates[:, None, :] * steps[None, :, None])
    local_part = jnp.sum(fall * prefix, axis=0)
    reach = weight[:, None, :] * jnp.exp(rates[:, None, :] * (last - steps)[None, :, None])
    local_part, reach = lax.optimization_barrier((local_part, reach))
    convolved = local_part + jnp.sum(reach * before[:, None, :], axis=0)
    conv_out = (convolved + skip_gain[None, :] * signal).astype(jnp.bfloat16)
    gated = (value_rows.astype(jnp.float32) * conv_out.astype(jnp.float32)).astype(jnp.bfloat16)

    heads_here = query_rows.shape[1] // HD
    previous_keys = shifted(key_rows, "ctx", 1)
    previous_gated = shifted(gated, "ctx", 1)
    key_window = jnp.concatenate([previous_keys, key_rows], axis=0).reshape(
        2 * row_count, heads_here, HD
    )
    value_window = jnp.concatenate([previous_gated, gated], axis=0).reshape(
        2 * row_count, heads_here, HD
    )
    query_heads = query_rows.reshape(row_count, heads_here, HD)
    scores = jnp.einsum(
        "qhd,khd->hqk", query_heads, key_window, preferred_element_type=jnp.float32
    ) * HD ** (-0.5)
    query_place = jnp.arange(row_count, dtype=jnp.int32)[:, None]
    key_place = jnp.arange(2 * row_count, dtype=jnp.int32)[None, :] - row_count
    allowed = (key_place <= query_place) & ((key_place >= 0) | (position > 0))
    scores = jnp.where(allowed[None], scores, -jnp.inf)
    row_max = jnp.max(scores, axis=-1, keepdims=True)
    weights = jnp.exp(scores - row_max)
    row_total = jnp.sum(weights, axis=-1)
    mixed_heads = jnp.einsum(
        "hqk,khd->qhd",
        weights.astype(jnp.bfloat16),
        value_window,
        preferred_element_type=jnp.float32,
    )
    mixed_heads = mixed_heads / jnp.transpose(row_total)[:, :, None]
    attention = mixed_heads.reshape(row_count, heads_here * HD).astype(jnp.bfloat16)
    attention_wide = attention.astype(jnp.float32)
    energy = jnp.sum(attention_wide * attention_wide, axis=1)
    total = energy
    for step in range(1, ch_count):
        total = total + rotated(energy, "ch", step)
    energy = total
    mean_square = energy / float(query_rows.shape[1] * ch_count)
    attended = (
        attention_wide * norm_gain[None, :] / jnp.sqrt(mean_square + 1e-06)[:, None]
    ).astype(jnp.bfloat16)
    return (conv_out, attended)


def solution(mesh):
    return jax.shard_map(
        per_device,
        mesh=mesh,
        in_specs=(
            P("ctx", "ch"),
            P("ch", None),
            P("ch", None),
            P("ch"),
            P("ctx", "ch"),
            P("ctx", "ch"),
            P("ctx", "ch"),
            P("ch"),
        ),
        out_specs=(P("ctx", "ch"), P("ctx", "ch")),
        check_vma=False,
    )
```

```python
import jax
import jax.numpy as jnp
from jax import lax
from jax.sharding import PartitionSpec as P

HD = 128


def shifted(block, axis, distance):
    devices = range(lax.axis_size(axis))
    route = [(i - distance, i) for i in devices if i - distance in devices]
    return lax.ppermute(block, axis, route)


def ramp(rates, sign, length, gain=None):
    fine_count = 16
    coarse_count = length // fine_count
    fine_t = jnp.arange(fine_count, dtype=jnp.float32)
    coarse_t = jnp.arange(coarse_count, dtype=jnp.float32) * float(fine_count)
    fine = jnp.exp(sign * rates[:, None, :] * fine_t[None, :, None])
    coarse = jnp.exp(sign * rates[:, None, :] * coarse_t[None, :, None])
    if gain is not None:
        coarse = coarse * gain[:, None, :]
    table = coarse[:, :, None, :] * fine[:, None, :, :]
    return table.reshape(rates.shape[0], length, rates.shape[1])


def per_device(
    conv_input, residues, decay_rates, skip_gain, query_rows, key_rows, value_rows, norm_gain
):
    ctx_count = lax.axis_size("ctx")
    ch_count = lax.axis_size("ch")
    position = lax.axis_index("ctx")
    row_count, chan_count = conv_input.shape
    signal = conv_input.astype(jnp.float32)
    rates = jnp.transpose(decay_rates)
    weight = jnp.transpose(residues) * jnp.sqrt(-jnp.expm1(-rates) * (1.0 + jnp.exp(-rates)))
    steps = jnp.arange(row_count, dtype=jnp.float32)
    last = float(row_count - 1)

    rise = ramp(rates, 1.0, row_count)
    lifted = rise * signal[None]
    own_state = jnp.exp(-rates * last) * jnp.sum(lifted, axis=1)

    before = jnp.zeros_like(own_state)
    span = 1
    while span < ctx_count:
        sent = own_state + before
        got = shifted(sent, "ctx", span)
        before = before + jnp.exp(-rates * float(row_count * span)) * got
        span *= 2

    lifted_hi = lifted.astype(jnp.bfloat16)
    lifted_lo = (lifted - lifted_hi.astype(jnp.float32)).astype(jnp.bfloat16)
    lower = (steps[:, None] >= steps[None, :]).astype(jnp.bfloat16)
    prefix = jnp.einsum(
        "ts,rsc->rtc", lower, lifted_hi, preferred_element_type=jnp.float32
    ) + jnp.einsum("ts,rsc->rtc", lower, lifted_lo, preferred_element_type=jnp.float32)

    fall = ramp(rates, -1.0, row_count, weight)
    local_part = jnp.sum(fall * prefix, axis=0)
    carried = jnp.exp(rates * last) * before
    convolved = local_part + jnp.sum(fall * carried[:, None, :], axis=0)
    conv_out = (convolved + skip_gain[None, :] * signal).astype(jnp.bfloat16)
    gated = (value_rows.astype(jnp.float32) * conv_out.astype(jnp.float32)).astype(jnp.bfloat16)

    heads_here = query_rows.shape[1] // HD
    previous_keys = shifted(key_rows, "ctx", 1)
    previous_gated = shifted(gated, "ctx", 1)
    key_window = jnp.concatenate([previous_keys, key_rows], axis=0).reshape(
        2 * row_count, heads_here, HD
    )
    value_window = jnp.concatenate([previous_gated, gated], axis=0).reshape(
        2 * row_count, heads_here, HD
    )
    query_heads = query_rows.reshape(row_count, heads_here, HD)
    scores = jnp.einsum(
        "qhd,khd->hqk", query_heads, key_window, preferred_element_type=jnp.float32
    ) * HD ** (-0.5)
    query_place = jnp.arange(row_count, dtype=jnp.int32)[:, None]
    key_place = jnp.arange(2 * row_count, dtype=jnp.int32)[None, :] - row_count
    allowed = (key_place <= query_place) & ((key_place >= 0) | (position > 0))
    scores = jnp.where(allowed[None], scores, -jnp.inf)
    row_max = jnp.max(scores, axis=-1, keepdims=True)
    weights = jnp.exp(scores - row_max)
    row_total = jnp.sum(weights, axis=-1)
    mixed_heads = jnp.einsum(
        "hqk,khd->qhd",
        weights.astype(jnp.bfloat16),
        value_window,
        preferred_element_type=jnp.float32,
    )
    mixed_heads = mixed_heads / jnp.transpose(row_total)[:, :, None]
    attention = mixed_heads.reshape(row_count, heads_here * HD).astype(jnp.bfloat16)
    attention_wide = attention.astype(jnp.float32)
    energy = jnp.sum(attention_wide * attention_wide, axis=1)
    spread = jnp.broadcast_to(energy[None, :], (ch_count, row_count))
    energy = jnp.sum(lax.all_to_all(spread, "ch", 0, 0, tiled=True), axis=0)
    mean_square = energy / float(query_rows.shape[1] * ch_count)
    attended = (
        attention_wide * norm_gain[None, :] / jnp.sqrt(mean_square + 1e-06)[:, None]
    ).astype(jnp.bfloat16)
    return (conv_out, attended)


def solution(mesh):
    return jax.shard_map(
        per_device,
        mesh=mesh,
        in_specs=(
            P("ctx", "ch"),
            P("ch", None),
            P("ch", None),
            P("ch"),
            P("ctx", "ch"),
            P("ctx", "ch"),
            P("ctx", "ch"),
            P("ch"),
        ),
        out_specs=(P("ctx", "ch"), P("ctx", "ch")),
        check_vma=False,
    )
```

```python
import jax
import jax.numpy as jnp
from jax import lax
from jax.sharding import PartitionSpec as P

HD = 128
TIE_SPAN = 4


def shifted(block, axis, distance):
    devices = range(lax.axis_size(axis))
    route = [(i - distance, i) for i in devices if i - distance in devices]
    return lax.ppermute(block, axis, route)


def ramp(rates, sign, length, gain=None):
    fine_count = 16
    coarse_count = length // fine_count
    fine_t = jnp.arange(fine_count, dtype=jnp.float32)
    coarse_t = jnp.arange(coarse_count, dtype=jnp.float32) * float(fine_count)
    fine = jnp.exp(sign * fine_t[:, None, None] * rates[None])
    coarse = jnp.exp(sign * coarse_t[:, None, None] * rates[None])
    if gain is not None:
        coarse = coarse * gain[None]
    table = coarse[:, None] * fine[None]
    return table.reshape((length,) + rates.shape)


def per_device(
    conv_input, residues, decay_rates, skip_gain, query_rows, key_rows, value_rows, norm_gain
):
    ctx_count = lax.axis_size("ctx")
    ch_count = lax.axis_size("ch")
    position = lax.axis_index("ctx")
    row_count, chan_count = conv_input.shape
    signal = conv_input.astype(jnp.float32)
    rates = jnp.transpose(decay_rates)
    weight = jnp.transpose(residues) * jnp.sqrt(-jnp.expm1(-rates) * (1.0 + jnp.exp(-rates)))
    steps = jnp.arange(row_count, dtype=jnp.float32)
    last = float(row_count - 1)

    rise = ramp(rates, 1.0, row_count)
    lifted = rise * signal[:, None, :]
    own_state = jnp.exp(-rates * last) * jnp.sum(lifted, axis=0)

    flat = lifted.reshape(row_count, -1)
    flat_hi = flat.astype(jnp.bfloat16)
    flat_lo = (flat - flat_hi.astype(jnp.float32)).astype(jnp.bfloat16)
    lower = (steps[:, None] >= steps[None, :]).astype(jnp.bfloat16)
    prefix = jnp.dot(lower, flat_hi, preferred_element_type=jnp.float32) + jnp.dot(
        lower, flat_lo, preferred_element_type=jnp.float32
    )
    fall = ramp(rates, -1.0, row_count, weight)
    local_part = jnp.sum(fall * prefix.reshape(lifted.shape), axis=1)

    before = jnp.zeros_like(own_state)
    span = 1
    while span < ctx_count:
        sent = own_state + before
        got = shifted(sent, "ctx", span)
        if span == TIE_SPAN:
            got, local_part = lax.optimization_barrier((got, local_part))
        before = before + jnp.exp(-rates * float(row_count * span)) * got
        span *= 2

    carried = jnp.exp(rates * last) * before
    convolved = local_part + jnp.sum(fall * carried[None], axis=1)
    conv_out = (convolved + skip_gain[None, :] * signal).astype(jnp.bfloat16)
    gated = (value_rows.astype(jnp.float32) * conv_out.astype(jnp.float32)).astype(jnp.bfloat16)

    heads_here = query_rows.shape[1] // HD
    previous_keys = shifted(key_rows, "ctx", 1)
    previous_gated = shifted(gated, "ctx", 1)
    key_window = jnp.concatenate([previous_keys, key_rows], axis=0).reshape(
        2 * row_count, heads_here, HD
    )
    value_window = jnp.concatenate([previous_gated, gated], axis=0).reshape(
        2 * row_count, heads_here, HD
    )
    query_heads = query_rows.reshape(row_count, heads_here, HD)
    scores = jnp.einsum(
        "qhd,khd->hqk", query_heads, key_window, preferred_element_type=jnp.float32
    ) * HD ** (-0.5)
    query_place = jnp.arange(row_count, dtype=jnp.int32)[:, None]
    key_place = jnp.arange(2 * row_count, dtype=jnp.int32)[None, :] - row_count
    allowed = (key_place <= query_place) & ((key_place >= 0) | (position > 0))
    scores = jnp.where(allowed[None], scores, -jnp.inf)
    row_max = jnp.max(scores, axis=-1, keepdims=True)
    weights = jnp.exp(scores - row_max)
    row_total = jnp.sum(weights, axis=-1)
    mixed_heads = jnp.einsum(
        "hqk,khd->qhd",
        weights.astype(jnp.bfloat16),
        value_window,
        preferred_element_type=jnp.float32,
    )
    mixed_heads = mixed_heads / jnp.transpose(row_total)[:, :, None]
    attention = mixed_heads.reshape(row_count, heads_here * HD).astype(jnp.bfloat16)
    attention_wide = attention.astype(jnp.float32)
    energy = jnp.sum(attention_wide * attention_wide, axis=1)
    spread = jnp.broadcast_to(energy[None, :], (ch_count, row_count))
    energy = jnp.sum(lax.all_to_all(spread, "ch", 0, 0, tiled=True), axis=0)
    mean_square = energy / float(query_rows.shape[1] * ch_count)
    attended = (
        attention_wide * norm_gain[None, :] / jnp.sqrt(mean_square + 1e-06)[:, None]
    ).astype(jnp.bfloat16)
    return (conv_out, attended)


def solution(mesh):
    return jax.shard_map(
        per_device,
        mesh=mesh,
        in_specs=(
            P("ctx", "ch"),
            P("ch", None),
            P("ch", None),
            P("ch"),
            P("ctx", "ch"),
            P("ctx", "ch"),
            P("ctx", "ch"),
            P("ch"),
        ),
        out_specs=(P("ctx", "ch"), P("ctx", "ch")),
        check_vma=False,
    )
```

```python
import jax
import jax.numpy as jnp
from jax import lax
from jax.sharding import PartitionSpec as P

HD = 128
TIE_SPAN = 4


def shifted(block, axis, distance):
    devices = range(lax.axis_size(axis))
    route = [(i - distance, i) for i in devices if i - distance in devices]
    return lax.ppermute(block, axis, route)


def per_device(
    conv_input, residues, decay_rates, skip_gain, query_rows, key_rows, value_rows, norm_gain
):
    ctx_count = lax.axis_size("ctx")
    ch_count = lax.axis_size("ch")
    position = lax.axis_index("ctx")
    row_count, chan_count = conv_input.shape
    signal = conv_input.astype(jnp.float32)
    rates = jnp.transpose(decay_rates)
    weight = jnp.transpose(residues) * jnp.sqrt(-jnp.expm1(-rates) * (1.0 + jnp.exp(-rates)))
    steps = jnp.arange(row_count, dtype=jnp.float32)
    last = float(row_count - 1)

    fine_count = 16
    fine_t = jnp.arange(fine_count, dtype=jnp.float32)
    coarse_t = jnp.arange(row_count // fine_count, dtype=jnp.float32) * float(fine_count)
    fine = jnp.exp(fine_t[:, None, None] * rates[None])
    coarse = jnp.exp(coarse_t[:, None, None] * rates[None])
    split_rows = signal.reshape(row_count // fine_count, fine_count, 1, chan_count)
    inner = jnp.sum(fine[None] * split_rows, axis=1)
    own_state = jnp.exp(-rates * last) * jnp.sum(coarse * inner, axis=0)

    lifted = jnp.exp(steps[:, None, None] * rates[None]) * signal[:, None, :]
    lifted_top = lax.reduce_precision(lifted, exponent_bits=8, mantissa_bits=7)
    lifted_hi = lifted_top.astype(jnp.bfloat16)
    lifted_lo = (lifted - lifted_top).astype(jnp.bfloat16)
    lower = (steps[:, None] >= steps[None, :]).astype(jnp.bfloat16)
    prefix = jnp.einsum(
        "ts,src->trc", lower, lifted_hi, preferred_element_type=jnp.float32
    ) + jnp.einsum("ts,src->trc", lower, lifted_lo, preferred_element_type=jnp.float32)
    fall = weight[None] * jnp.exp(-steps[:, None, None] * rates[None])
    local_part = jnp.sum(fall * prefix, axis=1)

    before = jnp.zeros_like(own_state)
    span = 1
    while span < ctx_count:
        sent = own_state + before
        got = shifted(sent, "ctx", span)
        if span == TIE_SPAN:
            got, local_part = lax.optimization_barrier((got, local_part))
        before = before + jnp.exp(-rates * float(row_count * span)) * got
        span *= 2

    carried = jnp.exp(rates * last) * before
    convolved = local_part + jnp.sum(fall * carried[None], axis=1)
    conv_out = (convolved + skip_gain[None, :] * signal).astype(jnp.bfloat16)
    gated = (value_rows.astype(jnp.float32) * conv_out.astype(jnp.float32)).astype(jnp.bfloat16)

    heads_here = query_rows.shape[1] // HD
    previous_keys = shifted(key_rows, "ctx", 1)
    previous_gated = shifted(gated, "ctx", 1)
    key_window = jnp.concatenate([previous_keys, key_rows], axis=0).reshape(
        2 * row_count, heads_here, HD
    )
    value_window = jnp.concatenate([previous_gated, gated], axis=0).reshape(
        2 * row_count, heads_here, HD
    )
    query_heads = query_rows.reshape(row_count, heads_here, HD)
    scores = jnp.einsum(
        "qhd,khd->hqk", query_heads, key_window, preferred_element_type=jnp.float32
    ) * HD ** (-0.5)
    query_place = jnp.arange(row_count, dtype=jnp.int32)[:, None]
    key_place = jnp.arange(2 * row_count, dtype=jnp.int32)[None, :] - row_count
    allowed = (key_place <= query_place) & ((key_place >= 0) | (position > 0))
    scores = jnp.where(allowed[None], scores, -jnp.inf)
    row_max = jnp.max(scores, axis=-1, keepdims=True)
    weights = jnp.exp(scores - row_max)
    row_total = jnp.sum(weights, axis=-1)
    mixed_heads = jnp.einsum(
        "hqk,khd->qhd",
        weights.astype(jnp.bfloat16),
        value_window,
        preferred_element_type=jnp.float32,
    )
    mixed_heads = mixed_heads / jnp.transpose(row_total)[:, :, None]
    attention = mixed_heads.reshape(row_count, heads_here * HD).astype(jnp.bfloat16)
    attention_wide = attention.astype(jnp.float32)
    energy = jnp.sum(attention_wide * attention_wide, axis=1)
    spread = jnp.broadcast_to(energy[None, :], (ch_count, row_count))
    energy = jnp.sum(lax.all_to_all(spread, "ch", 0, 0, tiled=True), axis=0)
    mean_square = energy / float(query_rows.shape[1] * ch_count)
    attended = (
        attention_wide * norm_gain[None, :] / jnp.sqrt(mean_square + 1e-06)[:, None]
    ).astype(jnp.bfloat16)
    return (conv_out, attended)


def solution(mesh):
    return jax.shard_map(
        per_device,
        mesh=mesh,
        in_specs=(
            P("ctx", "ch"),
            P("ch", None),
            P("ch", None),
            P("ch"),
            P("ctx", "ch"),
            P("ctx", "ch"),
            P("ctx", "ch"),
            P("ch"),
        ),
        out_specs=(P("ctx", "ch"), P("ctx", "ch")),
        check_vma=False,
    )
```

```python
import jax
import jax.numpy as jnp
from jax import lax
from jax.sharding import PartitionSpec as P

HD = 128
TIE_SPAN = 4


def shifted(block, axis, distance):
    devices = range(lax.axis_size(axis))
    route = [(i - distance, i) for i in devices if i - distance in devices]
    return lax.ppermute(block, axis, route)


def block_terms(signal, rates, weight, steps):
    row_count, chan_count = signal.shape
    last = float(row_count - 1)
    fine_count = 16
    fine_t = jnp.arange(fine_count, dtype=jnp.float32)
    coarse_t = jnp.arange(row_count // fine_count, dtype=jnp.float32) * float(fine_count)
    fine = jnp.exp(fine_t[:, None, None] * rates[None])
    coarse = jnp.exp(coarse_t[:, None, None] * rates[None])
    split_rows = signal.reshape(row_count // fine_count, fine_count, 1, chan_count)
    inner = jnp.sum(fine[None] * split_rows, axis=1)
    own_state = jnp.exp(-rates * last) * jnp.sum(coarse * inner, axis=0)

    lifted = jnp.exp(steps[:, None, None] * rates[None]) * signal[:, None, :]
    lifted_top = lax.reduce_precision(lifted, exponent_bits=8, mantissa_bits=7)
    lifted_hi = lifted_top.astype(jnp.bfloat16)
    lifted_lo = (lifted - lifted_top).astype(jnp.bfloat16)
    lower = (steps[:, None] >= steps[None, :]).astype(jnp.bfloat16)
    prefix = jnp.einsum(
        "ts,src->trc", lower, lifted_hi, preferred_element_type=jnp.float32
    ) + jnp.einsum("ts,src->trc", lower, lifted_lo, preferred_element_type=jnp.float32)
    fall = weight[None] * jnp.exp(-steps[:, None, None] * rates[None])
    local_part = jnp.sum(fall * prefix, axis=1)

    return own_state, fall, local_part


def per_device(
    conv_input, residues, decay_rates, skip_gain, query_rows, key_rows, value_rows, norm_gain
):
    ctx_count = lax.axis_size("ctx")
    ch_count = lax.axis_size("ch")
    position = lax.axis_index("ctx")
    row_count, chan_count = conv_input.shape
    signal = conv_input.astype(jnp.float32)
    rates = jnp.transpose(decay_rates)
    weight = jnp.transpose(residues) * jnp.sqrt(-jnp.expm1(-rates) * (1.0 + jnp.exp(-rates)))
    steps = jnp.arange(row_count, dtype=jnp.float32)
    last = float(row_count - 1)

    previous_signal = shifted(conv_input, "ctx", 1).astype(jnp.float32)
    previous_state, _, previous_local = block_terms(previous_signal, rates, weight, steps)
    own_state, fall, local_part = block_terms(signal, rates, weight, steps)
    lookback = shifted(jnp.stack([key_rows, value_rows]), "ctx", 1)
    previous_keys = lookback[0]

    before_previous = jnp.zeros_like(previous_state)
    span = 1
    while span < ctx_count:
        sent = previous_state + before_previous
        got = shifted(sent, "ctx", span)
        if span == TIE_SPAN:
            got, local_part = lax.optimization_barrier((got, local_part))
        if span == 2 * TIE_SPAN:
            got, previous_local = lax.optimization_barrier((got, previous_local))
        before_previous = before_previous + jnp.exp(-rates * float(row_count * span)) * got
        span *= 2
    before = jnp.exp(-rates * float(row_count)) * (previous_state + before_previous)

    carried = jnp.exp(rates * last) * before
    convolved = local_part + jnp.sum(fall * carried[None], axis=1)
    conv_out = (convolved + skip_gain[None, :] * signal).astype(jnp.bfloat16)
    gated = (value_rows.astype(jnp.float32) * conv_out.astype(jnp.float32)).astype(jnp.bfloat16)

    carried_previous = jnp.exp(rates * last) * before_previous
    convolved_previous = previous_local + jnp.sum(fall * carried_previous[None], axis=1)
    conv_previous = (convolved_previous + skip_gain[None, :] * previous_signal).astype(jnp.bfloat16)
    previous_gated = (
        lookback[1].astype(jnp.float32) * conv_previous.astype(jnp.float32)
    ).astype(jnp.bfloat16)

    heads_here = query_rows.shape[1] // HD
    key_window = jnp.concatenate([previous_keys, key_rows], axis=0).reshape(
        2 * row_count, heads_here, HD
    )
    value_window = jnp.concatenate([previous_gated, gated], axis=0).reshape(
        2 * row_count, heads_here, HD
    )
    query_heads = query_rows.reshape(row_count, heads_here, HD)
    scores = jnp.einsum(
        "qhd,khd->hqk", query_heads, key_window, preferred_element_type=jnp.float32
    ) * HD ** (-0.5)
    query_place = jnp.arange(row_count, dtype=jnp.int32)[:, None]
    key_place = jnp.arange(2 * row_count, dtype=jnp.int32)[None, :] - row_count
    allowed = (key_place <= query_place) & ((key_place >= 0) | (position > 0))
    scores = jnp.where(allowed[None], scores, -jnp.inf)
    row_max = jnp.max(scores, axis=-1, keepdims=True)
    weights = jnp.exp(scores - row_max)
    row_total = jnp.sum(weights, axis=-1)
    mixed_heads = jnp.einsum(
        "hqk,khd->qhd",
        weights.astype(jnp.bfloat16),
        value_window,
        preferred_element_type=jnp.float32,
    )
    mixed_heads = mixed_heads / jnp.transpose(row_total)[:, :, None]
    attention = mixed_heads.reshape(row_count, heads_here * HD).astype(jnp.bfloat16)
    attention_wide = attention.astype(jnp.float32)
    energy = jnp.sum(attention_wide * attention_wide, axis=1)
    spread = jnp.broadcast_to(energy[None, :], (ch_count, row_count))
    energy = jnp.sum(lax.all_to_all(spread, "ch", 0, 0, tiled=True), axis=0)
    mean_square = energy / float(query_rows.shape[1] * ch_count)
    attended = (
        attention_wide * norm_gain[None, :] / jnp.sqrt(mean_square + 1e-06)[:, None]
    ).astype(jnp.bfloat16)
    return (conv_out, attended)


def solution(mesh):
    return jax.shard_map(
        per_device,
        mesh=mesh,
        in_specs=(
            P("ctx", "ch"),
            P("ch", None),
            P("ch", None),
            P("ch"),
            P("ctx", "ch"),
            P("ctx", "ch"),
            P("ctx", "ch"),
            P("ch"),
        ),
        out_specs=(P("ctx", "ch"), P("ctx", "ch")),
        check_vma=False,
    )
```

```python
import jax
import jax.numpy as jnp
from jax import lax
from jax.sharding import PartitionSpec as P

HD = 128
TIE_SPAN = 4


def shifted(block, axis, distance):
    devices = range(lax.axis_size(axis))
    route = [(i - distance, i) for i in devices if i - distance in devices]
    return lax.ppermute(block, axis, route)


def block_terms(signal, rates, weight, steps):
    row_count, chan_count = signal.shape
    last = float(row_count - 1)
    fine_count = 16
    fine_t = jnp.arange(fine_count, dtype=jnp.float32)
    coarse_t = jnp.arange(row_count // fine_count, dtype=jnp.float32) * float(fine_count)
    fine = jnp.exp(fine_t[:, None, None] * rates[None])
    coarse = jnp.exp(coarse_t[:, None, None] * rates[None])
    split_rows = signal.reshape(row_count // fine_count, fine_count, 1, chan_count)
    inner = jnp.sum(fine[None] * split_rows, axis=1)
    own_state = jnp.exp(-rates * last) * jnp.sum(coarse * inner, axis=0)

    lifted = jnp.exp(steps[:, None, None] * rates[None]) * signal[:, None, :]
    lifted_top = lax.reduce_precision(lifted, exponent_bits=8, mantissa_bits=7)
    lifted_hi = lifted_top.astype(jnp.bfloat16)
    lifted_lo = (lifted - lifted_top).astype(jnp.bfloat16)
    lower = (steps[:, None] >= steps[None, :]).astype(jnp.bfloat16)
    prefix = jnp.einsum(
        "ts,src->trc", lower, lifted_hi, preferred_element_type=jnp.float32
    ) + jnp.einsum("ts,src->trc", lower, lifted_lo, preferred_element_type=jnp.float32)
    fall = weight[None] * jnp.exp(-steps[:, None, None] * rates[None])
    local_part = jnp.sum(fall * prefix, axis=1)

    return own_state, fall, local_part


def per_device(
    conv_input, residues, decay_rates, skip_gain, query_rows, key_rows, value_rows, norm_gain
):
    ctx_count = lax.axis_size("ctx")
    ch_count = lax.axis_size("ch")
    position = lax.axis_index("ctx")
    row_count, chan_count = conv_input.shape
    signal = conv_input.astype(jnp.float32)
    rates = jnp.transpose(decay_rates)
    weight = jnp.transpose(residues) * jnp.sqrt(-jnp.expm1(-rates) * (1.0 + jnp.exp(-rates)))
    steps = jnp.arange(row_count, dtype=jnp.float32)
    last = float(row_count - 1)

    previous_signal = shifted(conv_input, "ctx", 1).astype(jnp.float32)
    previous_state, _, previous_local = block_terms(previous_signal, rates, weight, steps)
    own_state, fall, local_part = block_terms(signal, rates, weight, steps)
    keys_values = jnp.stack([key_rows, value_rows])

    before_previous = jnp.zeros_like(previous_state)
    span = 1
    while span < ctx_count:
        sent = previous_state + before_previous
        got = shifted(sent, "ctx", span)
        if span == 1:
            got, keys_values = lax.optimization_barrier((got, keys_values))
            lookback = shifted(keys_values, "ctx", 1)
        if span == 4:
            got, lookback = lax.optimization_barrier((got, lookback))
        if span == TIE_SPAN:
            got, local_part = lax.optimization_barrier((got, local_part))
        if span == 2 * TIE_SPAN:
            got, previous_local = lax.optimization_barrier((got, previous_local))
        before_previous = before_previous + jnp.exp(-rates * float(row_count * span)) * got
        span *= 2
    before = jnp.exp(-rates * float(row_count)) * (previous_state + before_previous)
    previous_keys = lookback[0]

    carried = jnp.exp(rates * last) * before
    convolved = local_part + jnp.sum(fall * carried[None], axis=1)
    conv_out = (convolved + skip_gain[None, :] * signal).astype(jnp.bfloat16)
    gated = (value_rows.astype(jnp.float32) * conv_out.astype(jnp.float32)).astype(jnp.bfloat16)

    carried_previous = jnp.exp(rates * last) * before_previous
    convolved_previous = previous_local + jnp.sum(fall * carried_previous[None], axis=1)
    conv_previous = (convolved_previous + skip_gain[None, :] * previous_signal).astype(jnp.bfloat16)
    previous_gated = (
        lookback[1].astype(jnp.float32) * conv_previous.astype(jnp.float32)
    ).astype(jnp.bfloat16)

    heads_here = query_rows.shape[1] // HD
    key_window = jnp.concatenate([previous_keys, key_rows], axis=0).reshape(
        2 * row_count, heads_here, HD
    )
    value_window = jnp.concatenate([previous_gated, gated], axis=0).reshape(
        2 * row_count, heads_here, HD
    )
    query_heads = query_rows.reshape(row_count, heads_here, HD)
    scores = jnp.einsum(
        "qhd,khd->hqk", query_heads, key_window, preferred_element_type=jnp.float32
    ) * HD ** (-0.5)
    query_place = jnp.arange(row_count, dtype=jnp.int32)[:, None]
    key_place = jnp.arange(2 * row_count, dtype=jnp.int32)[None, :] - row_count
    allowed = (key_place <= query_place) & ((key_place >= 0) | (position > 0))
    scores = jnp.where(allowed[None], scores, -jnp.inf)
    row_max = jnp.max(scores, axis=-1, keepdims=True)
    weights = jnp.exp(scores - row_max)
    row_total = jnp.sum(weights, axis=-1)
    mixed_heads = jnp.einsum(
        "hqk,khd->qhd",
        weights.astype(jnp.bfloat16),
        value_window,
        preferred_element_type=jnp.float32,
    )
    mixed_heads = mixed_heads / jnp.transpose(row_total)[:, :, None]
    attention = mixed_heads.reshape(row_count, heads_here * HD).astype(jnp.bfloat16)
    attention_wide = attention.astype(jnp.float32)
    energy = jnp.sum(attention_wide * attention_wide, axis=1)
    spread = jnp.broadcast_to(energy[None, :], (ch_count, row_count))
    energy = jnp.sum(lax.all_to_all(spread, "ch", 0, 0, tiled=True), axis=0)
    mean_square = energy / float(query_rows.shape[1] * ch_count)
    attended = (
        attention_wide * norm_gain[None, :] / jnp.sqrt(mean_square + 1e-06)[:, None]
    ).astype(jnp.bfloat16)
    return (conv_out, attended)


def solution(mesh):
    return jax.shard_map(
        per_device,
        mesh=mesh,
        in_specs=(
            P("ctx", "ch"),
            P("ch", None),
            P("ch", None),
            P("ch"),
            P("ctx", "ch"),
            P("ctx", "ch"),
            P("ctx", "ch"),
            P("ch"),
        ),
        out_specs=(P("ctx", "ch"), P("ctx", "ch")),
        check_vma=False,
    )
```

```python
import jax
import jax.numpy as jnp
from jax import lax
from jax.sharding import PartitionSpec as P

HD = 128


def shifted(block, axis, distance):
    devices = range(lax.axis_size(axis))
    route = [(i - distance, i) for i in devices if i - distance in devices]
    return lax.ppermute(block, axis, route)


def block_terms(signal, rates, weight, steps):
    row_count, chan_count = signal.shape
    last = float(row_count - 1)
    fine_count = 16
    fine_t = jnp.arange(fine_count, dtype=jnp.float32)
    coarse_t = jnp.arange(row_count // fine_count, dtype=jnp.float32) * float(fine_count)
    fine = jnp.exp(fine_t[:, None, None] * rates[None])
    coarse = jnp.exp(coarse_t[:, None, None] * rates[None])
    split_rows = signal.reshape(row_count // fine_count, fine_count, 1, chan_count)
    inner = jnp.sum(fine[None] * split_rows, axis=1)
    own_state = jnp.exp(-rates * last) * jnp.sum(coarse * inner, axis=0)

    lifted = jnp.exp(steps[:, None, None] * rates[None]) * signal[:, None, :]
    lifted_top = lax.reduce_precision(lifted, exponent_bits=8, mantissa_bits=7)
    lifted_hi = lifted_top.astype(jnp.bfloat16)
    lifted_lo = (lifted - lifted_top).astype(jnp.bfloat16)
    lower = (steps[:, None] >= steps[None, :]).astype(jnp.bfloat16)
    prefix = jnp.einsum(
        "ts,src->trc", lower, lifted_hi, preferred_element_type=jnp.float32
    ) + jnp.einsum("ts,src->trc", lower, lifted_lo, preferred_element_type=jnp.float32)
    fall = weight[None] * jnp.exp(-steps[:, None, None] * rates[None])
    return own_state, fall, prefix


def per_device(
    conv_input, residues, decay_rates, skip_gain, query_rows, key_rows, value_rows, norm_gain
):
    ctx_count = lax.axis_size("ctx")
    ch_count = lax.axis_size("ch")
    position = lax.axis_index("ctx")
    row_count, chan_count = conv_input.shape
    signal = conv_input.astype(jnp.float32)
    rates = jnp.transpose(decay_rates)
    weight = jnp.transpose(residues) * jnp.sqrt(-jnp.expm1(-rates) * (1.0 + jnp.exp(-rates)))
    steps = jnp.arange(row_count, dtype=jnp.float32)
    last = float(row_count - 1)

    previous_signal = shifted(conv_input, "ctx", 1).astype(jnp.float32)
    previous_state, _, previous_prefix = block_terms(previous_signal, rates, weight, steps)
    own_state, fall, own_prefix = block_terms(signal, rates, weight, steps)
    keys_values = jnp.stack([key_rows, value_rows])

    before_previous = jnp.zeros_like(previous_state)
    span = 1
    while span < ctx_count:
        sent = previous_state + before_previous
        got = shifted(sent, "ctx", span)
        if span == 1:
            got, keys_values = lax.optimization_barrier((got, keys_values))
            lookback = shifted(keys_values, "ctx", 1)
        if span == 4:
            got, lookback = lax.optimization_barrier((got, lookback))
        if span == ctx_count // 8:
            got, previous_prefix = lax.optimization_barrier((got, previous_prefix))
            previous_local = jnp.sum(fall * previous_prefix, axis=1)
        if span == ctx_count // 4:
            got, previous_local, own_prefix = lax.optimization_barrier(
                (got, previous_local, own_prefix)
            )
            local_part = jnp.sum(fall * own_prefix, axis=1)
        if span == ctx_count // 2:
            got, local_part = lax.optimization_barrier((got, local_part))
        before_previous = before_previous + jnp.exp(-rates * float(row_count * span)) * got
        span *= 2
    before = jnp.exp(-rates * float(row_count)) * (previous_state + before_previous)
    previous_keys = lookback[0]

    carried = jnp.exp(rates * last) * before
    convolved = local_part + jnp.sum(fall * carried[None], axis=1)
    conv_out = (convolved + skip_gain[None, :] * signal).astype(jnp.bfloat16)
    gated = (value_rows.astype(jnp.float32) * conv_out.astype(jnp.float32)).astype(jnp.bfloat16)

    carried_previous = jnp.exp(rates * last) * before_previous
    convolved_previous = previous_local + jnp.sum(fall * carried_previous[None], axis=1)
    conv_previous = (convolved_previous + skip_gain[None, :] * previous_signal).astype(jnp.bfloat16)
    previous_gated = (
        lookback[1].astype(jnp.float32) * conv_previous.astype(jnp.float32)
    ).astype(jnp.bfloat16)

    heads_here = query_rows.shape[1] // HD
    key_window = jnp.concatenate([previous_keys, key_rows], axis=0).reshape(
        2 * row_count, heads_here, HD
    )
    value_window = jnp.concatenate([previous_gated, gated], axis=0).reshape(
        2 * row_count, heads_here, HD
    )
    query_heads = query_rows.reshape(row_count, heads_here, HD)
    scores = jnp.einsum(
        "qhd,khd->hqk", query_heads, key_window, preferred_element_type=jnp.float32
    ) * HD ** (-0.5)
    query_place = jnp.arange(row_count, dtype=jnp.int32)[:, None]
    key_place = jnp.arange(2 * row_count, dtype=jnp.int32)[None, :] - row_count
    allowed = (key_place <= query_place) & ((key_place >= 0) | (position > 0))
    scores = jnp.where(allowed[None], scores, -jnp.inf)
    row_max = jnp.max(scores, axis=-1, keepdims=True)
    weights = jnp.exp(scores - row_max)
    row_total = jnp.sum(weights, axis=-1)
    mixed_heads = jnp.einsum(
        "hqk,khd->qhd",
        weights.astype(jnp.bfloat16),
        value_window,
        preferred_element_type=jnp.float32,
    )
    mixed_heads = mixed_heads / jnp.transpose(row_total)[:, :, None]
    attention = mixed_heads.reshape(row_count, heads_here * HD).astype(jnp.bfloat16)
    attention_wide = attention.astype(jnp.float32)
    energy = jnp.sum(attention_wide * attention_wide, axis=1)
    spread = jnp.broadcast_to(energy[None, :], (ch_count, row_count))
    energy = jnp.sum(lax.all_to_all(spread, "ch", 0, 0, tiled=True), axis=0)
    mean_square = energy / float(query_rows.shape[1] * ch_count)
    attended = (
        attention_wide * norm_gain[None, :] / jnp.sqrt(mean_square + 1e-06)[:, None]
    ).astype(jnp.bfloat16)
    return (conv_out, attended)


def solution(mesh):
    return jax.shard_map(
        per_device,
        mesh=mesh,
        in_specs=(
            P("ctx", "ch"),
            P("ch", None),
            P("ch", None),
            P("ch"),
            P("ctx", "ch"),
            P("ctx", "ch"),
            P("ctx", "ch"),
            P("ch"),
        ),
        out_specs=(P("ctx", "ch"), P("ctx", "ch")),
        check_vma=False,
    )
```

```python
import jax
import jax.numpy as jnp
from jax import lax
from jax.sharding import PartitionSpec as P

HD = 128


def shifted(block, axis, distance):
    devices = range(lax.axis_size(axis))
    route = [(i - distance, i) for i in devices if i - distance in devices]
    return lax.ppermute(block, axis, route)


def block_terms(signal, rates, weight, steps):
    row_count, chan_count = signal.shape
    last = float(row_count - 1)
    fine_count = 16
    fine_t = jnp.arange(fine_count, dtype=jnp.float32)
    coarse_t = jnp.arange(row_count // fine_count, dtype=jnp.float32) * float(fine_count)
    fine = jnp.exp(fine_t[:, None, None] * rates[None])
    coarse = jnp.exp(coarse_t[:, None, None] * rates[None])
    split_rows = signal.reshape(row_count // fine_count, fine_count, 1, chan_count)
    inner = jnp.sum(fine[None] * split_rows, axis=1)
    own_state = jnp.exp(-rates * last) * jnp.sum(coarse * inner, axis=0)

    lifted = jnp.exp(steps[:, None, None] * rates[None]) * signal[:, None, :]
    lifted_top = lax.reduce_precision(lifted, exponent_bits=8, mantissa_bits=7)
    lifted_hi = lifted_top.astype(jnp.bfloat16)
    lifted_lo = (lifted - lifted_top).astype(jnp.bfloat16)
    lower = (steps[:, None] >= steps[None, :]).astype(jnp.bfloat16)
    prefix = jnp.einsum(
        "ts,src->trc", lower, lifted_hi, preferred_element_type=jnp.float32
    ) + jnp.einsum("ts,src->trc", lower, lifted_lo, preferred_element_type=jnp.float32)
    fall = weight[None] * jnp.exp(-steps[:, None, None] * rates[None])
    return own_state, fall, prefix


def per_device(
    conv_input, residues, decay_rates, skip_gain, query_rows, key_rows, value_rows, norm_gain
):
    ctx_count = lax.axis_size("ctx")
    ch_count = lax.axis_size("ch")
    position = lax.axis_index("ctx")
    row_count, chan_count = conv_input.shape
    signal = conv_input.astype(jnp.float32)
    rates = jnp.transpose(decay_rates)
    weight = jnp.transpose(residues) * jnp.sqrt(-jnp.expm1(-rates) * (1.0 + jnp.exp(-rates)))
    steps = jnp.arange(row_count, dtype=jnp.float32)
    last = float(row_count - 1)

    previous_signal = shifted(conv_input, "ctx", 1).astype(jnp.float32)
    previous_state, _, previous_prefix = block_terms(previous_signal, rates, weight, steps)
    own_state, fall, own_prefix = block_terms(signal, rates, weight, steps)
    keys_values = jnp.stack([key_rows, value_rows])

    before_previous = jnp.zeros_like(previous_state)
    previous_local = local_part = None
    span = 1
    while span < ctx_count:
        sent = previous_state + before_previous
        reach = 4 if span * 4 == ctx_count else 2
        got = jnp.zeros_like(sent)
        for step in range(1, reach):
            decay = jnp.exp(-rates * float(row_count * span * step))
            got = got + decay * shifted(sent, "ctx", step * span)
        if span == 1:
            got, keys_values = lax.optimization_barrier((got, keys_values))
            lookback = shifted(keys_values, "ctx", 1)
        if span == ctx_count // 16:
            got, lookback, previous_prefix = lax.optimization_barrier(
                (got, lookback, previous_prefix)
            )
            previous_local = jnp.sum(fall * previous_prefix, axis=1)
        if span == ctx_count // 8:
            got, previous_local, own_prefix = lax.optimization_barrier(
                (got, previous_local, own_prefix)
            )
            local_part = jnp.sum(fall * own_prefix, axis=1)
        if span == ctx_count // 4:
            got, local_part = lax.optimization_barrier((got, local_part))
        before_previous = before_previous + got
        span *= reach
    if previous_local is None:
        previous_local = jnp.sum(fall * previous_prefix, axis=1)
    if local_part is None:
        local_part = jnp.sum(fall * own_prefix, axis=1)
    before = jnp.exp(-rates * float(row_count)) * (previous_state + before_previous)
    previous_keys = lookback[0]

    carried = jnp.exp(rates * last) * before
    convolved = local_part + jnp.sum(fall * carried[None], axis=1)
    conv_out = (convolved + skip_gain[None, :] * signal).astype(jnp.bfloat16)
    gated = (value_rows.astype(jnp.float32) * conv_out.astype(jnp.float32)).astype(jnp.bfloat16)

    carried_previous = jnp.exp(rates * last) * before_previous
    convolved_previous = previous_local + jnp.sum(fall * carried_previous[None], axis=1)
    conv_previous = (convolved_previous + skip_gain[None, :] * previous_signal).astype(jnp.bfloat16)
    previous_gated = (
        lookback[1].astype(jnp.float32) * conv_previous.astype(jnp.float32)
    ).astype(jnp.bfloat16)

    heads_here = query_rows.shape[1] // HD
    key_window = jnp.concatenate([previous_keys, key_rows], axis=0).reshape(
        2 * row_count, heads_here, HD
    )
    value_window = jnp.concatenate([previous_gated, gated], axis=0).reshape(
        2 * row_count, heads_here, HD
    )
    query_heads = query_rows.reshape(row_count, heads_here, HD)
    scores = jnp.einsum(
        "qhd,khd->hqk", query_heads, key_window, preferred_element_type=jnp.float32
    ) * HD ** (-0.5)
    query_place = jnp.arange(row_count, dtype=jnp.int32)[:, None]
    key_place = jnp.arange(2 * row_count, dtype=jnp.int32)[None, :] - row_count
    allowed = (key_place <= query_place) & ((key_place >= 0) | (position > 0))
    scores = jnp.where(allowed[None], scores, -jnp.inf)
    row_max = jnp.max(scores, axis=-1, keepdims=True)
    weights = jnp.exp(scores - row_max)
    row_total = jnp.sum(weights, axis=-1)
    mixed_heads = jnp.einsum(
        "hqk,khd->qhd",
        weights.astype(jnp.bfloat16),
        value_window,
        preferred_element_type=jnp.float32,
    )
    mixed_heads = mixed_heads / jnp.transpose(row_total)[:, :, None]
    attention = mixed_heads.reshape(row_count, heads_here * HD).astype(jnp.bfloat16)
    attention_wide = attention.astype(jnp.float32)
    energy = jnp.sum(attention_wide * attention_wide, axis=1)
    spread = jnp.broadcast_to(energy[None, :], (ch_count, row_count))
    energy = jnp.sum(lax.all_to_all(spread, "ch", 0, 0, tiled=True), axis=0)
    mean_square = energy / float(query_rows.shape[1] * ch_count)
    attended = (
        attention_wide * norm_gain[None, :] / jnp.sqrt(mean_square + 1e-06)[:, None]
    ).astype(jnp.bfloat16)
    return (conv_out, attended)


def solution(mesh):
    return jax.shard_map(
        per_device,
        mesh=mesh,
        in_specs=(
            P("ctx", "ch"),
            P("ch", None),
            P("ch", None),
            P("ch"),
            P("ctx", "ch"),
            P("ctx", "ch"),
            P("ctx", "ch"),
            P("ch"),
        ),
        out_specs=(P("ctx", "ch"), P("ctx", "ch")),
        check_vma=False,
    )
```

```python
import jax
import jax.numpy as jnp
from jax import lax
from jax.sharding import PartitionSpec as P

HD = 128


def shifted(block, axis, distance):
    devices = range(lax.axis_size(axis))
    route = [(i - distance, i) for i in devices if i - distance in devices]
    return lax.ppermute(block, axis, route)


def block_terms(signal, rates, weight, steps):
    row_count, chan_count = signal.shape
    last = float(row_count - 1)
    fine_count = 16
    fine_t = jnp.arange(fine_count, dtype=jnp.float32)
    coarse_t = jnp.arange(row_count // fine_count, dtype=jnp.float32) * float(fine_count)
    fine = jnp.exp(fine_t[:, None, None] * rates[None])
    coarse = jnp.exp(coarse_t[:, None, None] * rates[None])
    split_rows = signal.reshape(row_count // fine_count, fine_count, 1, chan_count)
    inner = jnp.sum(fine[None] * split_rows, axis=1)
    own_state = jnp.exp(-rates * last) * jnp.sum(coarse * inner, axis=0)

    lifted = jnp.exp(steps[:, None, None] * rates[None]) * signal[:, None, :]
    lifted_top = lax.reduce_precision(lifted, exponent_bits=8, mantissa_bits=7)
    lifted_hi = lifted_top.astype(jnp.bfloat16)
    lifted_lo = (lifted - lifted_top).astype(jnp.bfloat16)
    lower = (steps[:, None] >= steps[None, :]).astype(jnp.bfloat16)
    prefix = jnp.einsum(
        "ts,src->trc", lower, lifted_hi, preferred_element_type=jnp.float32
    ) + jnp.einsum("ts,src->trc", lower, lifted_lo, preferred_element_type=jnp.float32)
    fall = weight[None] * jnp.exp(-steps[:, None, None] * rates[None])
    return own_state, fall, prefix


def per_device(
    conv_input, residues, decay_rates, skip_gain, query_rows, key_rows, value_rows, norm_gain
):
    ctx_count = lax.axis_size("ctx")
    ch_count = lax.axis_size("ch")
    position = lax.axis_index("ctx")
    row_count, chan_count = conv_input.shape
    signal = conv_input.astype(jnp.float32)
    rates = jnp.transpose(decay_rates)
    weight = jnp.transpose(residues) * jnp.sqrt(-jnp.expm1(-rates) * (1.0 + jnp.exp(-rates)))
    steps = jnp.arange(row_count, dtype=jnp.float32)
    last = float(row_count - 1)

    previous_signal = shifted(conv_input, "ctx", 1).astype(jnp.float32)
    previous_state, _, previous_prefix = block_terms(previous_signal, rates, weight, steps)
    own_state, fall, own_prefix = block_terms(signal, rates, weight, steps)
    keys_values = jnp.stack([key_rows, value_rows])

    before_previous = jnp.zeros_like(previous_state)
    previous_local = local_part = None
    span = 1
    while span < ctx_count:
        sent = previous_state + before_previous
        reach = 4 if span >= 4 and span * 4 <= ctx_count else 2
        parts = [shifted(sent, "ctx", step * span) for step in range(1, reach)]
        got = parts[0]
        if span == 1:
            got, keys_values = lax.optimization_barrier((got, keys_values))
            lookback = shifted(keys_values, "ctx", 1)
        if span == ctx_count // 32:
            got, lookback, previous_prefix = lax.optimization_barrier(
                (got, lookback, previous_prefix)
            )
            previous_local = jnp.sum(fall * previous_prefix, axis=1)
        if span == ctx_count // 16:
            got, previous_local, own_prefix = lax.optimization_barrier(
                (got, previous_local, own_prefix)
            )
            local_part = jnp.sum(fall * own_prefix, axis=1)
        if span == ctx_count // 4:
            got, local_part = lax.optimization_barrier((got, local_part))
        parts[0] = got
        for step in range(1, reach):
            decay = jnp.exp(-rates * float(row_count * span * step))
            before_previous = before_previous + decay * parts[step - 1]
        span *= reach
    if previous_local is None:
        previous_local = jnp.sum(fall * previous_prefix, axis=1)
    if local_part is None:
        local_part = jnp.sum(fall * own_prefix, axis=1)
    before = jnp.exp(-rates * float(row_count)) * (previous_state + before_previous)
    previous_keys = lookback[0]

    carried = jnp.exp(rates * last) * before
    convolved = local_part + jnp.sum(fall * carried[None], axis=1)
    conv_out = (convolved + skip_gain[None, :] * signal).astype(jnp.bfloat16)
    gated = (value_rows.astype(jnp.float32) * conv_out.astype(jnp.float32)).astype(jnp.bfloat16)

    carried_previous = jnp.exp(rates * last) * before_previous
    convolved_previous = previous_local + jnp.sum(fall * carried_previous[None], axis=1)
    conv_previous = (convolved_previous + skip_gain[None, :] * previous_signal).astype(jnp.bfloat16)
    previous_gated = (
        lookback[1].astype(jnp.float32) * conv_previous.astype(jnp.float32)
    ).astype(jnp.bfloat16)

    heads_here = query_rows.shape[1] // HD
    key_window = jnp.concatenate([previous_keys, key_rows], axis=0).reshape(
        2 * row_count, heads_here, HD
    )
    value_window = jnp.concatenate([previous_gated, gated], axis=0).reshape(
        2 * row_count, heads_here, HD
    )
    query_heads = query_rows.reshape(row_count, heads_here, HD)
    scores = jnp.einsum(
        "qhd,khd->hqk", query_heads, key_window, preferred_element_type=jnp.float32
    ) * HD ** (-0.5)
    query_place = jnp.arange(row_count, dtype=jnp.int32)[:, None]
    key_place = jnp.arange(2 * row_count, dtype=jnp.int32)[None, :] - row_count
    allowed = (key_place <= query_place) & ((key_place >= 0) | (position > 0))
    scores = jnp.where(allowed[None], scores, -jnp.inf)
    row_max = jnp.max(scores, axis=-1, keepdims=True)
    weights = jnp.exp(scores - row_max)
    row_total = jnp.sum(weights, axis=-1)
    mixed_heads = jnp.einsum(
        "hqk,khd->qhd",
        weights.astype(jnp.bfloat16),
        value_window,
        preferred_element_type=jnp.float32,
    )
    mixed_heads = mixed_heads / jnp.transpose(row_total)[:, :, None]
    attention = mixed_heads.reshape(row_count, heads_here * HD).astype(jnp.bfloat16)
    attention_wide = attention.astype(jnp.float32)
    energy = jnp.sum(attention_wide * attention_wide, axis=1)
    spread = jnp.broadcast_to(energy[None, :], (ch_count, row_count))
    energy = jnp.sum(lax.all_to_all(spread, "ch", 0, 0, tiled=True), axis=0)
    mean_square = energy / float(query_rows.shape[1] * ch_count)
    attended = (
        attention_wide * norm_gain[None, :] / jnp.sqrt(mean_square + 1e-06)[:, None]
    ).astype(jnp.bfloat16)
    return (conv_out, attended)


def solution(mesh):
    return jax.shard_map(
        per_device,
        mesh=mesh,
        in_specs=(
            P("ctx", "ch"),
            P("ch", None),
            P("ch", None),
            P("ch"),
            P("ctx", "ch"),
            P("ctx", "ch"),
            P("ctx", "ch"),
            P("ch"),
        ),
        out_specs=(P("ctx", "ch"), P("ctx", "ch")),
        check_vma=False,
    )
```

```python
import jax
import jax.numpy as jnp
from jax import lax
from jax.sharding import PartitionSpec as P

HD = 128


def shifted(block, axis, distance):
    devices = range(lax.axis_size(axis))
    route = [(i - distance, i) for i in devices if i - distance in devices]
    return lax.ppermute(block, axis, route)


def block_terms(signal, rates, weight, steps):
    row_count, chan_count = signal.shape
    last = float(row_count - 1)
    fine_count = 16
    fine_t = jnp.arange(fine_count, dtype=jnp.float32)
    coarse_t = jnp.arange(row_count // fine_count, dtype=jnp.float32) * float(fine_count)
    fine = jnp.exp(fine_t[:, None, None] * rates[None])
    coarse = jnp.exp(coarse_t[:, None, None] * rates[None])
    split_rows = signal.reshape(row_count // fine_count, fine_count, 1, chan_count)
    inner = jnp.sum(fine[None] * split_rows, axis=1)
    own_state = jnp.exp(-rates * last) * jnp.sum(coarse * inner, axis=0)

    lifted = jnp.exp(steps[:, None, None] * rates[None]) * signal[:, None, :]
    lifted_top = lax.reduce_precision(lifted, exponent_bits=8, mantissa_bits=7)
    lifted_hi = lifted_top.astype(jnp.bfloat16)
    lifted_lo = (lifted - lifted_top).astype(jnp.bfloat16)
    lower = (steps[:, None] >= steps[None, :]).astype(jnp.bfloat16)
    prefix = jnp.einsum(
        "ts,src->trc", lower, lifted_hi, preferred_element_type=jnp.float32
    ) + jnp.einsum("ts,src->trc", lower, lifted_lo, preferred_element_type=jnp.float32)
    fall = weight[None] * jnp.exp(-steps[:, None, None] * rates[None])
    return own_state, fall, prefix


def per_device(
    conv_input, residues, decay_rates, skip_gain, query_rows, key_rows, value_rows, norm_gain
):
    ctx_count = lax.axis_size("ctx")
    ch_count = lax.axis_size("ch")
    position = lax.axis_index("ctx")
    row_count, chan_count = conv_input.shape
    signal = conv_input.astype(jnp.float32)
    rates = jnp.transpose(decay_rates)
    weight = jnp.transpose(residues) * jnp.sqrt(-jnp.expm1(-rates) * (1.0 + jnp.exp(-rates)))
    steps = jnp.arange(row_count, dtype=jnp.float32)
    last = float(row_count - 1)

    previous_signal = shifted(conv_input, "ctx", 1).astype(jnp.float32)
    previous_state, _, previous_prefix = block_terms(previous_signal, rates, weight, steps)
    own_state, fall, own_prefix = block_terms(signal, rates, weight, steps)
    keys_values = jnp.stack([key_rows, value_rows])

    before_previous = jnp.zeros_like(previous_state)
    previous_local = local_part = None
    span = 1
    while span < ctx_count:
        sent = previous_state + before_previous
        reach = 4 if span * 4 == ctx_count else 2
        got = jnp.zeros_like(sent)
        for step in sorted(range(1, reach), key=lambda k: -min(k, reach - k)):
            decay = jnp.exp(-rates * float(row_count * span * step))
            got = got + decay * shifted(sent, "ctx", step * span)
        if span == 1:
            got, keys_values = lax.optimization_barrier((got, keys_values))
            lookback = shifted(keys_values, "ctx", 1)
        if span == ctx_count // 16:
            got, lookback, previous_prefix = lax.optimization_barrier(
                (got, lookback, previous_prefix)
            )
            previous_local = jnp.sum(fall * previous_prefix, axis=1)
        if span == ctx_count // 8:
            got, previous_local, own_prefix = lax.optimization_barrier(
                (got, previous_local, own_prefix)
            )
            local_part = jnp.sum(fall * own_prefix, axis=1)
        if span == ctx_count // 4:
            got, local_part = lax.optimization_barrier((got, local_part))
        before_previous = before_previous + got
        span *= reach
    if previous_local is None:
        previous_local = jnp.sum(fall * previous_prefix, axis=1)
    if local_part is None:
        local_part = jnp.sum(fall * own_prefix, axis=1)
    before = jnp.exp(-rates * float(row_count)) * (previous_state + before_previous)
    previous_keys = lookback[0]

    carried = jnp.exp(rates * last) * before
    convolved = local_part + jnp.sum(fall * carried[None], axis=1)
    conv_out = (convolved + skip_gain[None, :] * signal).astype(jnp.bfloat16)
    gated = (value_rows.astype(jnp.float32) * conv_out.astype(jnp.float32)).astype(jnp.bfloat16)

    carried_previous = jnp.exp(rates * last) * before_previous
    convolved_previous = previous_local + jnp.sum(fall * carried_previous[None], axis=1)
    conv_previous = (convolved_previous + skip_gain[None, :] * previous_signal).astype(jnp.bfloat16)
    previous_gated = (
        lookback[1].astype(jnp.float32) * conv_previous.astype(jnp.float32)
    ).astype(jnp.bfloat16)

    heads_here = query_rows.shape[1] // HD
    key_window = jnp.concatenate([previous_keys, key_rows], axis=0).reshape(
        2 * row_count, heads_here, HD
    )
    value_window = jnp.concatenate([previous_gated, gated], axis=0).reshape(
        2 * row_count, heads_here, HD
    )
    query_heads = query_rows.reshape(row_count, heads_here, HD)
    scores = jnp.einsum(
        "qhd,khd->hqk", query_heads, key_window, preferred_element_type=jnp.float32
    ) * HD ** (-0.5)
    query_place = jnp.arange(row_count, dtype=jnp.int32)[:, None]
    key_place = jnp.arange(2 * row_count, dtype=jnp.int32)[None, :] - row_count
    allowed = (key_place <= query_place) & ((key_place >= 0) | (position > 0))
    scores = jnp.where(allowed[None], scores, -jnp.inf)
    row_max = jnp.max(scores, axis=-1, keepdims=True)
    weights = jnp.exp(scores - row_max)
    row_total = jnp.sum(weights, axis=-1)
    mixed_heads = jnp.einsum(
        "hqk,khd->qhd",
        weights.astype(jnp.bfloat16),
        value_window,
        preferred_element_type=jnp.float32,
    )
    mixed_heads = mixed_heads / jnp.transpose(row_total)[:, :, None]
    attention = mixed_heads.reshape(row_count, heads_here * HD).astype(jnp.bfloat16)
    attention_wide = attention.astype(jnp.float32)
    energy = jnp.sum(attention_wide * attention_wide, axis=1)
    spread = jnp.broadcast_to(energy[None, :], (ch_count, row_count))
    energy = jnp.sum(lax.all_to_all(spread, "ch", 0, 0, tiled=True), axis=0)
    mean_square = energy / float(query_rows.shape[1] * ch_count)
    attended = (
        attention_wide * norm_gain[None, :] / jnp.sqrt(mean_square + 1e-06)[:, None]
    ).astype(jnp.bfloat16)
    return (conv_out, attended)


def solution(mesh):
    return jax.shard_map(
        per_device,
        mesh=mesh,
        in_specs=(
            P("ctx", "ch"),
            P("ch", None),
            P("ch", None),
            P("ch"),
            P("ctx", "ch"),
            P("ctx", "ch"),
            P("ctx", "ch"),
            P("ch"),
        ),
        out_specs=(P("ctx", "ch"), P("ctx", "ch")),
        check_vma=False,
    )
```

```python
import jax
import jax.numpy as jnp
from jax import lax
from jax.sharding import PartitionSpec as P

HD = 128


def shifted(block, axis, distance):
    devices = range(lax.axis_size(axis))
    route = [(i - distance, i) for i in devices if i - distance in devices]
    return lax.ppermute(block, axis, route)


def block_terms(signal, rates, weight, steps):
    row_count, chan_count = signal.shape
    last = float(row_count - 1)
    fine_count = 16
    fine_t = jnp.arange(fine_count, dtype=jnp.float32)
    coarse_t = jnp.arange(row_count // fine_count, dtype=jnp.float32) * float(fine_count)
    fine = jnp.exp(fine_t[:, None, None] * rates[None])
    coarse = jnp.exp(coarse_t[:, None, None] * rates[None])
    split_rows = signal.reshape(row_count // fine_count, fine_count, 1, chan_count)
    inner = jnp.sum(fine[None] * split_rows, axis=1)
    own_state = jnp.exp(-rates * last) * jnp.sum(coarse * inner, axis=0)

    lifted = jnp.exp(steps[:, None, None] * rates[None]) * signal[:, None, :]
    lifted_top = lax.reduce_precision(lifted, exponent_bits=8, mantissa_bits=7)
    lifted_hi = lifted_top.astype(jnp.bfloat16)
    lifted_lo = (lifted - lifted_top).astype(jnp.bfloat16)
    lower = (steps[:, None] >= steps[None, :]).astype(jnp.bfloat16)
    prefix = jnp.einsum(
        "ts,src->trc", lower, lifted_hi, preferred_element_type=jnp.float32
    ) + jnp.einsum("ts,src->trc", lower, lifted_lo, preferred_element_type=jnp.float32)
    fall = weight[None] * jnp.exp(-steps[:, None, None] * rates[None])
    return own_state, fall, prefix


def per_device(
    conv_input, residues, decay_rates, skip_gain, query_rows, key_rows, value_rows, norm_gain
):
    ctx_count = lax.axis_size("ctx")
    ch_count = lax.axis_size("ch")
    position = lax.axis_index("ctx")
    row_count, chan_count = conv_input.shape
    signal = conv_input.astype(jnp.float32)
    rates = jnp.transpose(decay_rates)
    weight = jnp.transpose(residues) * jnp.sqrt(-jnp.expm1(-rates) * (1.0 + jnp.exp(-rates)))
    steps = jnp.arange(row_count, dtype=jnp.float32)
    last = float(row_count - 1)

    previous_signal = shifted(conv_input, "ctx", 1).astype(jnp.float32)
    previous_state, _, previous_prefix = block_terms(previous_signal, rates, weight, steps)
    own_state, fall, own_prefix = block_terms(signal, rates, weight, steps)
    keys_values = jnp.stack([key_rows, value_rows])

    before_previous = jnp.zeros_like(previous_state)
    previous_local = local_part = None
    span = 1
    while span < ctx_count:
        sent = previous_state + before_previous
        reach = 4 if span * 4 == ctx_count else 2
        got = jnp.zeros_like(sent)
        for step in sorted(range(1, reach), key=lambda k: -min(k, reach - k)):
            decay = jnp.exp(-rates * float(row_count * span * step))
            got = got + decay * shifted(sent, "ctx", step * span)
        if span == 2:
            got, keys_values = lax.optimization_barrier((got, keys_values))
            lookback = shifted(keys_values, "ctx", 1)
        if span == ctx_count // 16:
            got, lookback, previous_prefix = lax.optimization_barrier(
                (got, lookback, previous_prefix)
            )
            previous_local = jnp.sum(fall * previous_prefix, axis=1)
        if span == ctx_count // 8:
            got, previous_local, own_prefix = lax.optimization_barrier(
                (got, previous_local, own_prefix)
            )
            local_part = jnp.sum(fall * own_prefix, axis=1)
        if span == ctx_count // 4:
            got, local_part = lax.optimization_barrier((got, local_part))
        before_previous = before_previous + got
        span *= reach
    if previous_local is None:
        previous_local = jnp.sum(fall * previous_prefix, axis=1)
    if local_part is None:
        local_part = jnp.sum(fall * own_prefix, axis=1)
    before = jnp.exp(-rates * float(row_count)) * (previous_state + before_previous)
    previous_keys = lookback[0]

    carried = jnp.exp(rates * last) * before
    convolved = local_part + jnp.sum(fall * carried[None], axis=1)
    conv_out = (convolved + skip_gain[None, :] * signal).astype(jnp.bfloat16)
    gated = (value_rows.astype(jnp.float32) * conv_out.astype(jnp.float32)).astype(jnp.bfloat16)

    carried_previous = jnp.exp(rates * last) * before_previous
    convolved_previous = previous_local + jnp.sum(fall * carried_previous[None], axis=1)
    conv_previous = (convolved_previous + skip_gain[None, :] * previous_signal).astype(jnp.bfloat16)
    previous_gated = (
        lookback[1].astype(jnp.float32) * conv_previous.astype(jnp.float32)
    ).astype(jnp.bfloat16)

    heads_here = query_rows.shape[1] // HD
    key_window = jnp.concatenate([previous_keys, key_rows], axis=0).reshape(
        2 * row_count, heads_here, HD
    )
    value_window = jnp.concatenate([previous_gated, gated], axis=0).reshape(
        2 * row_count, heads_here, HD
    )
    query_heads = query_rows.reshape(row_count, heads_here, HD)
    scores = jnp.einsum(
        "qhd,khd->hqk", query_heads, key_window, preferred_element_type=jnp.float32
    ) * HD ** (-0.5)
    query_place = jnp.arange(row_count, dtype=jnp.int32)[:, None]
    key_place = jnp.arange(2 * row_count, dtype=jnp.int32)[None, :] - row_count
    allowed = (key_place <= query_place) & ((key_place >= 0) | (position > 0))
    scores = jnp.where(allowed[None], scores, -jnp.inf)
    row_max = jnp.max(scores, axis=-1, keepdims=True)
    weights = jnp.exp(scores - row_max)
    row_total = jnp.sum(weights, axis=-1)
    mixed_heads = jnp.einsum(
        "hqk,khd->qhd",
        weights.astype(jnp.bfloat16),
        value_window,
        preferred_element_type=jnp.float32,
    )
    mixed_heads = mixed_heads / jnp.transpose(row_total)[:, :, None]
    attention = mixed_heads.reshape(row_count, heads_here * HD).astype(jnp.bfloat16)
    attention_wide = attention.astype(jnp.float32)
    energy = jnp.sum(attention_wide * attention_wide, axis=1)
    spread = jnp.broadcast_to(energy[None, :], (ch_count, row_count))
    energy = jnp.sum(lax.all_to_all(spread, "ch", 0, 0, tiled=True), axis=0)
    mean_square = energy / float(query_rows.shape[1] * ch_count)
    attended = (
        attention_wide * norm_gain[None, :] / jnp.sqrt(mean_square + 1e-06)[:, None]
    ).astype(jnp.bfloat16)
    return (conv_out, attended)


def solution(mesh):
    return jax.shard_map(
        per_device,
        mesh=mesh,
        in_specs=(
            P("ctx", "ch"),
            P("ch", None),
            P("ch", None),
            P("ch"),
            P("ctx", "ch"),
            P("ctx", "ch"),
            P("ctx", "ch"),
            P("ch"),
        ),
        out_specs=(P("ctx", "ch"), P("ctx", "ch")),
        check_vma=False,
    )
```
